256 devices in a mesh: seq: 32 (over x, z), head: 8 (over y, core).
Axes of the slice: x: 4, y: 4, z: 8, core: 2. Of those that a mesh axis runs over, the one named last changes fastest.
Arguments:
- queries: bfloat16 [4, 8192, 2048], P(None, 'seq', 'head'), may hold values from -6 to 6
- keys: bfloat16 [4, 8192, 2048], P(None, 'seq', 'head'), may hold values from -6 to 6
- values: bfloat16 [4, 8192, 2048], P(None, 'seq', 'head'), may hold values from -6 to 6
- out_grad: bfloat16 [4, 8192, 2048], P(None, ('seq', 'head')), may hold values from -6 to 6
- selected: int32 [4, 32, 16, 2], P(None, None, 'head'), may hold values from 0 to 63, as said below
Outputs:
- attended: bfloat16 [4, 8192, 2048], P(None, 'seq', 'head')
- query_gradient: bfloat16 [4, 8192, 2048], P(None, 'seq', 'head')
- key_grad: bfloat16 [4, 8192, 2048], P(None, 'seq', 'head')
- value_grad: bfloat16 [4, 8192, 2048], P(None, 'seq', 'head')
The draws below stay inside these ranges and needn't reach their ends.
Inputs may be any that keep to these rules, and one draw needn't show every extreme that they name: selected[f, s, h, j] selects for head h an earlier block of the query block that device s holds in slice f (block s // 2, 31 - s // 2, 32 + s // 2, 63 - s // 2 for f = 0, 1, 2, 3); an entry not smaller than that block's number selects nothing. Rows 2 m and 2 m + 1 are equal. Let the group of block b be r or 31 - r, whichever is smaller, with r = b mod 32. For one head and one m, the usable entries of the four query blocks lie in different groups, none of them group m.
All inputs are finite; a program needn't handle non-finite values.
Results may differ from the reference program's by a relative error of at most 0.0074.
Values may be sent and summed in bfloat16 or wider, within the bound.
No kernel may reach another device: no remote copies, remote signals or barrier semaphores. Data moves between devices by JAX's collectives and lax.ppermute only.
A program may use at most 128 MiB of HBM per device.

```python
import math
import jax
import jax.numpy as jnp
from jax import lax

HD = 128
HEADS = 16
BLK = 512
TOPK = 2
HALF = 256
BLOCKS = 64
N_SEQ = 32


def draw_selected(key, part):
    groups = N_SEQ // 2
    others = groups - 1
    slots = 4 * TOPK
    taken = min(slots, others)
    streams = jax.random.split(key, 3)
    group_ids = jnp.arange(groups, dtype=jnp.int32)[:, None, None]
    rank_ids = jnp.arange(others, dtype=jnp.int32)[None, None, :]
    group_of = rank_ids + (rank_ids >= group_ids).astype(jnp.int32)
    group_of = jnp.broadcast_to(group_of, (groups, HEADS, others))
    noise = jax.random.randint(streams[0], (groups, HEADS, others), 0, 2 * others)
    ranking = (noise + group_of) * groups + group_of
    order = jnp.argsort(ranking, axis=-1)[:, :, :taken]
    picked = jnp.take_along_axis(group_of, order, axis=-1)
    gvec = jnp.arange(groups, dtype=jnp.int32)
    query_blocks = jnp.stack([gvec, N_SEQ - 1 - gvec, N_SEQ + gvec, 2 * N_SEQ - 1 - gvec], axis=1)
    query_row = jnp.arange(taken, dtype=jnp.int32) // TOPK
    query_of_slot = query_blocks[:, query_row][:, None, :]
    candidates = jnp.stack([picked, N_SEQ - 1 - picked, N_SEQ + picked, 2 * N_SEQ - 1 - picked], axis=-1)
    allowed = jnp.sum((candidates < query_of_slot[..., None]).astype(jnp.int32), axis=-1)
    shape = (groups, HEADS, taken)
    hot = jax.random.randint(streams[1], shape, 0, 2)
    pick_any = jax.random.randint(streams[2], shape, 0, jnp.maximum(allowed, 1))
    index = jnp.where(hot == 1, 0, pick_any)
    block = jnp.take_along_axis(candidates, index[..., None], axis=-1)[..., 0]
    block = jnp.where(allowed > 0, block, 2 * N_SEQ - 1)
    filler = jnp.full((groups, HEADS, slots - taken), 2 * N_SEQ - 1, dtype=jnp.int32)
    full_rows = jnp.concatenate([block, filler], axis=-1)
    per_group = full_rows.reshape(groups, HEADS, 4, TOPK).transpose(2, 0, 1, 3)
    return jnp.repeat(per_group, 2, axis=1).astype(jnp.int32)


def drawn_pair(key):
    rows = N_SEQ * HALF
    shape = (4, rows, HEADS, HD)
    streams = jax.random.split(key, 2)
    query_vals = jnp.clip(jax.random.normal(streams[0], shape), -4.0, 4.0)
    key_vals = jnp.clip(jax.random.normal(streams[1], shape), -4.0, 4.0)
    return (query_vals.reshape(4, rows, HEADS * HD).astype(jnp.bfloat16), key_vals.reshape(4, rows, HEADS * HD).astype(jnp.bfloat16))


def draw_queries(key, part):
    return drawn_pair(jax.random.fold_in(key, 7))[0]


def draw_keys(key, part):
    return drawn_pair(jax.random.fold_in(key, 7))[1]


def levels(rng, dims, shards, smallest, top_value):
    level, own = 1.0, jax.random.fold_in(rng, 6)
    for position, blocks in shards:
        heights = jnp.exp(jax.random.uniform(jax.random.fold_in(own, position), (blocks,), jnp.float32, smallest / len(shards), top_value / len(shards)))
        level = level * jnp.repeat(heights, dims[position] // blocks).reshape([-1 if axis == position else 1 for axis in range(len(dims))])
    return level


def bell_draw(stream_key, dims, deviation, reach, cuts=(), held_as=jnp.bfloat16):
    drawn = jax.random.normal(stream_key, dims, jnp.float32) * deviation
    if len(cuts) > 0:
        drawn = levels(stream_key, dims, cuts, -0.22, 0.18) * drawn
    return jnp.clip(drawn, min=-reach, max=reach).astype(held_as)


def setup_inputs(seed: int = 0) -> dict:
    key_list = jax.random.split(jax.random.key(seed), 6)
    queries = draw_queries(jax.random.fold_in(key_list[5], 71), 0)
    keys = draw_keys(jax.random.fold_in(key_list[5], 71), 0)
    values = bell_draw(key_list[2], (4, N_SEQ * HALF, HEADS * HD), 1.0, 6.0, ((1, 32), (2, 8)))
    out_grad = bell_draw(key_list[3], (4, N_SEQ * HALF, HEADS * HD), 1.0, 6.0, ((1, 256),))
    selected = draw_selected(jax.random.fold_in(key_list[5], 71), 0)
    return {"queries": queries, "keys": keys, "values": values, "out_grad": out_grad, "selected": selected}


def to_blocks(stored):
    width = stored.shape[2]
    pieces = []
    for slice_id in range(4):
        span_rows = stored[slice_id].reshape(N_SEQ, HALF, width)
        if slice_id % 2 == 1:
            span_rows = span_rows[::-1]
        pieces.append(span_rows)
    return jnp.concatenate(pieces, axis=0).reshape(BLOCKS, BLK, width)

def to_stored(blocks):
    width = blocks.shape[2]
    spans = blocks.reshape(4 * N_SEQ, HALF, width)
    pieces = []
    for slice_id in range(4):
        part_rows = spans[slice_id * N_SEQ:(slice_id + 1) * N_SEQ]
        if slice_id % 2 == 1:
            part_rows = part_rows[::-1]
        pieces.append(part_rows.reshape(N_SEQ * HALF, width))
    return jnp.stack(pieces, axis=0)

def split_heads(stored):
    blocks = to_blocks(stored)
    return blocks.reshape(BLOCKS, BLK, HEADS, HD).transpose(2, 0, 1, 3)

def merge_heads(split):
    blocks = split.transpose(1, 2, 0, 3).reshape(BLOCKS, BLK, HEADS * HD)
    return to_stored(blocks)

def combine(terms, choice_ids, usable):
    own_first = terms[:, 0, :HALF] + lax.optimization_barrier(terms[:, 1, :HALF].astype(jnp.bfloat16)).astype(jnp.float32)
    own_second = terms[:, 1, HALF:BLK]
    own_part = jnp.concatenate([own_first, own_second], axis=1)
    picked = terms[:, :, BLK:].reshape(BLOCKS, 2, TOPK, BLK, HD)
    items = lax.optimization_barrier(picked.astype(jnp.bfloat16)).astype(jnp.float32)
    segments = jnp.where(usable[:, None, :], choice_ids[:, None, :], BLOCKS)
    segments = jnp.broadcast_to(segments, (BLOCKS, 2, TOPK)).reshape(BLOCKS * 2 * TOPK).astype(jnp.int32)
    summed = jax.ops.segment_sum(items.reshape(BLOCKS * 2 * TOPK, BLK, HD), segments, num_segments=BLOCKS + 1)[:BLOCKS]
    return own_part + summed

def one_head(operands):
    q_block, k_block, v_block, g_block, choice_ids = operands
    logit_scale_factor = 1.0 / math.sqrt(HD)
    block_ids = jnp.arange(BLOCKS, dtype=jnp.int32)
    usable = choice_ids < block_ids[:, None]
    safe_ids = jnp.where(usable, choice_ids, 0).astype(jnp.int32)
    every_key_row = jnp.concatenate([k_block, k_block[safe_ids[:, 0]], k_block[safe_ids[:, 1]]], axis=1).astype(jnp.float32)
    every_value_row = jnp.concatenate([v_block, v_block[safe_ids[:, 0]], v_block[safe_ids[:, 1]]], axis=1).astype(jnp.float32)
    query_wide = q_block.astype(jnp.float32)
    output_grad_wide = g_block.astype(jnp.float32)
    attention_logits = jnp.einsum('vwt,vmt->vwm', query_wide, every_key_row) * logit_scale_factor
    places = jnp.arange(BLK, dtype=jnp.int32)
    own_vis = places[None, :] <= places[:, None]
    visible = jnp.concatenate([jnp.broadcast_to(own_vis[None], (BLOCKS, BLK, BLK)), jnp.broadcast_to(usable[:, 0, None, None], (BLOCKS, BLK, BLK)), jnp.broadcast_to(usable[:, 1, None, None], (BLOCKS, BLK, BLK))], axis=2)
    masked = jnp.where(visible, attention_logits, -jnp.inf)
    row_max = lax.optimization_barrier(jnp.max(masked, axis=-1, keepdims=True))
    exp_vals = jnp.exp(masked - row_max)
    probs = exp_vals / lax.optimization_barrier(jnp.sum(exp_vals, axis=-1, keepdims=True))
    probability_narrow = probs.astype(jnp.bfloat16).astype(jnp.float32)
    attended = jnp.einsum('jmz,jzs->jms', probability_narrow, every_value_row).astype(jnp.bfloat16)
    probability_gradient = jnp.einsum('vwt,vmt->vwm', output_grad_wide, every_value_row)
    row_delta = lax.optimization_barrier(jnp.sum(probs * probability_gradient, axis=-1, keepdims=True))
    score_gradient = (probs * (probability_gradient - row_delta)).astype(jnp.bfloat16).astype(jnp.float32)
    query_gradient = (logit_scale_factor * jnp.einsum('jmz,jzs->jms', score_gradient, every_key_row)).astype(jnp.bfloat16)
    grad_halves = score_gradient.reshape(BLOCKS, 2, HALF, 3 * BLK)
    prob_halves = probability_narrow.reshape(BLOCKS, 2, HALF, 3 * BLK)
    key_terms = logit_scale_factor * jnp.einsum('bhqk,bhqd->bhkd', grad_halves, query_wide.reshape(BLOCKS, 2, HALF, HD))
    value_terms = jnp.einsum('bhqk,bhqd->bhkd', prob_halves, output_grad_wide.reshape(BLOCKS, 2, HALF, HD))
    key_grad = combine(key_terms, choice_ids, usable).astype(jnp.bfloat16)
    value_grad = combine(value_terms, choice_ids, usable).astype(jnp.bfloat16)
    return (attended, query_gradient, key_grad, value_grad)

def reference(queries, keys, values, out_grad, selected):
    q_heads = split_heads(queries)
    k_heads = split_heads(keys)
    v_heads = split_heads(values)
    g_heads = split_heads(out_grad)
    pieces = []
    for slice_id in range(4):
        sel_rows = selected[slice_id, 0::2]
        if slice_id % 2 == 1:
            sel_rows = sel_rows[::-1]
        pieces.append(sel_rows)
    block_sel = jnp.concatenate(pieces, axis=0).transpose(1, 0, 2)
    attended, query_gradient, key_grad, value_grad = lax.map(one_head, (q_heads, k_heads, v_heads, g_heads, block_sel))
    return (merge_heads(attended), merge_heads(query_gradient), merge_heads(key_grad), merge_heads(value_grad))
```

```python
import math

import jax
import jax.numpy as jnp
from jax import lax
from jax.sharding import Mesh, PartitionSpec as P

HD = 128


def swap_pair(value):
    return lax.ppermute(value, "sp", [(0, 1), (1, 0)])


def per_head(stored, head_count):
    slices = stored.shape[0]
    rows = stored.shape[1]
    return stored.reshape(slices, rows, head_count, HD).transpose(2, 0, 1, 3)


def merge_heads(split):
    head_count = split.shape[0]
    slices = split.shape[1]
    rows = split.shape[2]
    return split.transpose(1, 2, 0, 3).reshape(slices, rows, head_count * HD)


def local(queries, keys, values, out_grad, selected):
    groups = lax.axis_size("sg")
    seq_count = 2 * groups
    group_id = lax.axis_index("sg")
    parity = lax.axis_index("sp")
    slices = queries.shape[0]
    half_len = queries.shape[1]
    block_len = 2 * half_len
    head_count = queries.shape[2] // HD
    logit_scale_factor = 1.0 / math.sqrt(HD)
    q_heads = per_head(queries, head_count)
    k_heads = per_head(keys, head_count)
    v_heads = per_head(values, head_count)
    grad_rows = lax.all_to_all(out_grad, "head", split_axis=2, concat_axis=1, tiled=True)
    g_heads = per_head(grad_rows, head_count)
    kv = jnp.stack([k_heads, v_heads])

    sel_g = selected[:, 0::2]
    gid = jnp.arange(groups, dtype=jnp.int32)
    query_block = jnp.stack([gid, seq_count - 1 - gid, seq_count + gid, 2 * seq_count - 1 - gid])
    usable_g = sel_g < query_block[:, :, None, None]
    mine_block = jnp.stack(
        [group_id, seq_count - 1 - group_id, seq_count + group_id, 2 * seq_count - 1 - group_id]
    )
    hits = usable_g[..., None] & (sel_g[..., None] == mine_block)
    need = jnp.any(hits, axis=(0, 3)).astype(jnp.bfloat16)
    mine_sel = lax.dynamic_index_in_dim(sel_g, group_id, 1, keepdims=False)
    mine_usable = mine_sel < mine_block[:, None, None]
    fold = mine_sel % seq_count
    src_group = jnp.where(fold >= groups, seq_count - 1 - fold, fold)
    src_group = jnp.where(mine_usable, src_group, 0)

    send = jnp.einsum(
        "ghf,chfld->gchld", need, kv, preferred_element_type=jnp.float32
    ).astype(jnp.bfloat16)
    got = lax.all_to_all(send, "sg", split_axis=0, concat_axis=0, tiled=True)
    got_h = got.transpose(2, 0, 1, 3, 4)
    head_index = jnp.arange(head_count, dtype=jnp.int32)[None, :, None]
    taken = got_h[head_index, src_group]
    held_half = (jnp.arange(slices, dtype=jnp.int32) + parity) % 2
    pairs_kv = kv.reshape(2, head_count, slices // 2, 2, half_len, HD)
    lead = jnp.where(parity == 0, pairs_kv[:, :, :, 0], pairs_kv[:, :, :, 1])
    other, mate = swap_pair((taken, lead))

    empty_span = jnp.zeros((2, head_count, half_len, HD), jnp.bfloat16)
    own_rows = []
    for slice_id in range(slices):
        second = jnp.concatenate([mate[:, :, slice_id // 2], kv[:, :, slice_id]], axis=2)
        first = jnp.concatenate([kv[:, :, slice_id], empty_span], axis=2)
        own_rows.append(jnp.where(held_half[slice_id] == 1, second, first))
    own_kv = jnp.stack(own_rows, axis=0)
    sel_kv = jnp.stack([taken, other], axis=3)
    sel_kv = sel_kv.transpose(0, 4, 1, 2, 3, 5, 6).reshape(
        slices, 2, head_count, 2 * sel_g.shape[3] * half_len, HD
    )
    every_kv = jnp.concatenate([own_kv, sel_kv], axis=3)

    key_pos = jnp.arange(block_len, dtype=jnp.int32)
    query_pos = held_half[:, None] * half_len + jnp.arange(half_len, dtype=jnp.int32)[None, :]
    own_vis = key_pos[None, None, :] <= query_pos[:, :, None]
    sel_vis = jnp.repeat(mine_usable, block_len, axis=2)
    visible = jnp.concatenate(
        [
            jnp.broadcast_to(own_vis[:, None], (slices, head_count, half_len, block_len)),
            jnp.broadcast_to(
                sel_vis[:, :, None, :], (slices, head_count, half_len, sel_vis.shape[2])
            ),
        ],
        axis=-1,
    )

    def attend(operands):
        q_one, k_one, v_one, g_one, vis_one = operands
        attention_logits = (
            jnp.einsum("hqd,hkd->hqk", q_one, k_one, preferred_element_type=jnp.float32)
            * logit_scale_factor
        )
        masked = jnp.where(vis_one, attention_logits, -jnp.inf)
        row_max = jnp.max(masked, axis=-1, keepdims=True)
        exp_vals = jnp.exp(masked - row_max)
        probs = exp_vals / jnp.sum(exp_vals, axis=-1, keepdims=True)
        probability_narrow = probs.astype(jnp.bfloat16)
        attended = jnp.einsum(
            "hqk,hkd->hqd", probability_narrow, v_one, preferred_element_type=jnp.float32
        ).astype(jnp.bfloat16)
        probability_gradient = jnp.einsum(
            "hqd,hkd->hqk", g_one, v_one, preferred_element_type=jnp.float32
        )
        row_delta = jnp.sum(probs * probability_gradient, axis=-1, keepdims=True)
        score_gradient = (probs * (probability_gradient - row_delta)).astype(jnp.bfloat16)
        query_gradient = (
            logit_scale_factor
            * jnp.einsum("hqk,hkd->hqd", score_gradient, k_one, preferred_element_type=jnp.float32)
        ).astype(jnp.bfloat16)
        key_terms = logit_scale_factor * jnp.einsum(
            "hqk,hqd->hkd", score_gradient, q_one, preferred_element_type=jnp.float32
        )
        value_terms = jnp.einsum(
            "hqk,hqd->hkd", probability_narrow, g_one, preferred_element_type=jnp.float32
        )
        return (attended, query_gradient, jnp.stack([key_terms, value_terms]))

    attended, query_gradient, terms = lax.map(
        attend,
        (
            jnp.moveaxis(q_heads, 1, 0),
            every_kv[:, 0],
            every_kv[:, 1],
            jnp.moveaxis(g_heads, 1, 0),
            visible,
        ),
    )

    sel_terms = terms[:, :, :, block_len:].reshape(
        slices, 2, head_count, sel_g.shape[3], 2, half_len, HD
    )
    mine_terms = sel_terms[:, :, :, :, 0]
    other_terms = sel_terms[:, :, :, :, 1].astype(jnp.bfloat16)
    by_pair = terms[:, :, :, :half_len].reshape(slices // 2, 2, 2, head_count, half_len, HD)
    trail = jnp.where(parity == 0, by_pair[:, 1], by_pair[:, 0]).astype(jnp.bfloat16)
    partner_terms, mate_back = swap_pair((other_terms, trail))
    summed = (mine_terms + partner_terms.astype(jnp.float32)).astype(jnp.bfloat16)
    route = (
        (src_group[None] == gid[:, None, None, None]) & mine_usable[None]
    ).astype(jnp.bfloat16)
    send_back = jnp.einsum(
        "gfhj,fchjld->gchld", route, summed, preferred_element_type=jnp.float32
    ).astype(jnp.bfloat16)
    back = lax.all_to_all(send_back, "sg", split_axis=0, concat_axis=0, tiled=True)
    gathered = jnp.einsum("ghf,gchld->chfld", need, back, preferred_element_type=jnp.float32)

    def own_part(kind):
        rows_kept = []
        for slice_id in range(slices):
            first = terms[slice_id, kind, :, :half_len] + mate_back[slice_id // 2, kind].astype(
                jnp.float32
            )
            second = terms[slice_id, kind, :, half_len:block_len]
            rows_kept.append(jnp.where(held_half[slice_id] == 0, first, second))
        return jnp.stack(rows_kept, axis=1)

    key_grad = (own_part(0) + gathered[0]).astype(jnp.bfloat16)
    value_grad = (own_part(1) + gathered[1]).astype(jnp.bfloat16)
    attended_rows = attended.transpose(0, 2, 1, 3).reshape(slices, half_len, head_count * HD)
    query_rows = query_gradient.transpose(0, 2, 1, 3).reshape(slices, half_len, head_count * HD)
    return (attended_rows, query_rows, merge_heads(key_grad), merge_heads(value_grad))


def solution(mesh):
    seq_count = mesh.shape["seq"]
    head_count = mesh.shape["head"]
    pair_mesh = Mesh(
        mesh.devices.reshape(seq_count // 2, 2, head_count), ("sg", "sp", "head")
    )
    tokens = P(None, ("sg", "sp"), "head")
    in_specs = (
        tokens,
        tokens,
        tokens,
        P(None, ("sg", "sp", "head"), None),
        P(None, None, "head", None),
    )
    out_specs = (tokens, tokens, tokens, tokens)
    return jax.shard_map(local, mesh=pair_mesh, in_specs=in_specs, out_specs=out_specs, check_vma=False)
```

```python
import math

import jax
import jax.numpy as jnp
from jax import lax
from jax.sharding import Mesh, PartitionSpec as P

HD = 128


def swap_pair(value):
    return lax.ppermute(value, "sp", [(0, 1), (1, 0)])


def per_head(stored, head_count):
    slices = stored.shape[0]
    rows = stored.shape[1]
    return stored.reshape(slices, rows, head_count, HD).transpose(2, 0, 1, 3)


def merge_heads(split):
    head_count = split.shape[0]
    slices = split.shape[1]
    rows = split.shape[2]
    return split.transpose(1, 2, 0, 3).reshape(slices, rows, head_count * HD)


def local(queries, keys, values, out_grad, selected):
    groups = lax.axis_size("sg")
    seq_count = 2 * groups
    group_id = lax.axis_index("sg")
    parity = lax.axis_index("sp")
    slices = queries.shape[0]
    half_len = queries.shape[1]
    block_len = 2 * half_len
    head_count = queries.shape[2] // HD
    logit_scale_factor = 1.0 / math.sqrt(HD)
    q_heads = per_head(queries, head_count)
    k_heads = per_head(keys, head_count)
    v_heads = per_head(values, head_count)
    grad_rows = lax.all_to_all(out_grad, "head", split_axis=2, concat_axis=1, tiled=True)
    g_heads = per_head(grad_rows, head_count)
    kv = jnp.stack([k_heads, v_heads])

    sel_g = selected[:, 0::2]
    gid = jnp.arange(groups, dtype=jnp.int32)
    query_block = jnp.stack([gid, seq_count - 1 - gid, seq_count + gid, 2 * seq_count - 1 - gid])
    usable_g = sel_g < query_block[:, :, None, None]
    mine_block = jnp.stack(
        [group_id, seq_count - 1 - group_id, seq_count + group_id, 2 * seq_count - 1 - group_id]
    )
    hits = usable_g[..., None] & (sel_g[..., None] == mine_block)
    need = jnp.any(hits, axis=(0, 3)).astype(jnp.bfloat16)
    mine_sel = lax.dynamic_index_in_dim(sel_g, group_id, 1, keepdims=False)
    mine_usable = mine_sel < mine_block[:, None, None]
    fold = mine_sel % seq_count
    src_group = jnp.where(fold >= groups, seq_count - 1 - fold, fold)
    src_group = jnp.where(mine_usable, src_group, 0)

    send = jnp.einsum(
        "ghf,chfld->gchld", need, kv, preferred_element_type=jnp.float32
    ).astype(jnp.bfloat16)
    held_half = (jnp.arange(slices, dtype=jnp.int32) + parity) % 2
    pairs_kv = kv.reshape(2, head_count, slices // 2, 2, half_len, HD)
    lead = jnp.where(parity == 0, pairs_kv[:, :, :, 0], pairs_kv[:, :, :, 1])
    mate = swap_pair(lead)

    empty_span = jnp.zeros((2, head_count, half_len, HD), jnp.bfloat16)
    own_rows = []
    for slice_id in range(slices):
        second = jnp.concatenate([mate[:, :, slice_id // 2], kv[:, :, slice_id]], axis=2)
        first = jnp.concatenate([kv[:, :, slice_id], empty_span], axis=2)
        own_rows.append(jnp.where(held_half[slice_id] == 1, second, first))
    own_kv = jnp.stack(own_rows, axis=0)

    key_pos = jnp.arange(block_len, dtype=jnp.int32)
    query_pos = held_half[:, None] * half_len + jnp.arange(half_len, dtype=jnp.int32)[None, :]
    own_vis = key_pos[None, None, :] <= query_pos[:, :, None]
    sel_vis = jnp.repeat(mine_usable, block_len, axis=2)
    topk = sel_g.shape[3]

    def attend(operands):
        q_one, k_one, v_one, g_one, vis_one = operands
        attention_logits = (
            jnp.einsum("qd,kd->qk", q_one, k_one, preferred_element_type=jnp.float32)
            * logit_scale_factor
        )
        masked = jnp.where(vis_one, attention_logits, -jnp.inf)
        row_max = jnp.max(masked, axis=-1, keepdims=True)
        exp_vals = jnp.exp(masked - row_max)
        probs = exp_vals / jnp.sum(exp_vals, axis=-1, keepdims=True)
        probability_narrow = probs.astype(jnp.bfloat16)
        attended = jnp.einsum(
            "qk,kd->qd", probability_narrow, v_one, preferred_element_type=jnp.float32
        ).astype(jnp.bfloat16)
        probability_gradient = jnp.einsum(
            "qd,kd->qk", g_one, v_one, preferred_element_type=jnp.float32
        )
        row_delta = jnp.sum(probs * probability_gradient, axis=-1, keepdims=True)
        score_gradient = (probs * (probability_gradient - row_delta)).astype(jnp.bfloat16)
        query_gradient = (
            logit_scale_factor
            * jnp.einsum("qk,kd->qd", score_gradient, k_one, preferred_element_type=jnp.float32)
        ).astype(jnp.bfloat16)
        key_terms = logit_scale_factor * jnp.einsum(
            "qk,qd->kd", score_gradient, q_one, preferred_element_type=jnp.float32
        )
        value_terms = jnp.einsum(
            "qk,qd->kd", probability_narrow, g_one, preferred_element_type=jnp.float32
        )
        return (attended, query_gradient, jnp.stack([key_terms, value_terms]))

    attended_heads = []
    query_heads = []
    key_heads = []
    value_heads = []
    for head in range(head_count):
        got = lax.all_to_all(send[:, :, head], "sg", split_axis=0, concat_axis=0, tiled=True)
        taken = got[src_group[:, head]]
        other = swap_pair(taken)
        sel_kv = jnp.stack([taken, other], axis=2)
        sel_kv = sel_kv.transpose(0, 3, 1, 2, 4, 5).reshape(
            slices, 2, 2 * topk * half_len, HD
        )
        every_kv = jnp.concatenate([own_kv[:, :, head], sel_kv], axis=2)
        visible = jnp.concatenate(
            [
                own_vis,
                jnp.broadcast_to(
                    sel_vis[:, head, None, :], (slices, half_len, sel_vis.shape[2])
                ),
            ],
            axis=-1,
        )
        attended, query_gradient, terms = lax.map(
            attend,
            (q_heads[head], every_kv[:, 0], every_kv[:, 1], g_heads[head], visible),
        )
        sel_terms = terms[:, :, block_len:].reshape(slices, 2, topk, 2, half_len, HD)
        mine_terms = sel_terms[:, :, :, 0]
        other_terms = sel_terms[:, :, :, 1].astype(jnp.bfloat16)
        by_pair = terms[:, :, :half_len].reshape(slices // 2, 2, 2, half_len, HD)
        trail = jnp.where(parity == 0, by_pair[:, 1], by_pair[:, 0]).astype(jnp.bfloat16)
        partner_terms, mate_back = swap_pair((other_terms, trail))
        summed = (mine_terms + partner_terms.astype(jnp.float32)).astype(jnp.bfloat16)
        route = (
            (src_group[None, :, head] == gid[:, None, None]) & mine_usable[None, :, head]
        ).astype(jnp.bfloat16)
        send_back = jnp.einsum(
            "gfj,fcjld->gcld", route, summed, preferred_element_type=jnp.float32
        ).astype(jnp.bfloat16)
        back = lax.all_to_all(send_back, "sg", split_axis=0, concat_axis=0, tiled=True)
        gathered = jnp.einsum(
            "gf,gcld->cfld", need[:, head], back, preferred_element_type=jnp.float32
        )
        rows_kept = []
        for slice_id in range(slices):
            first = terms[slice_id, :, :half_len] + mate_back[slice_id // 2].astype(jnp.float32)
            second = terms[slice_id, :, half_len:block_len]
            rows_kept.append(jnp.where(held_half[slice_id] == 0, first, second))
        grads = (jnp.stack(rows_kept, axis=1) + gathered).astype(jnp.bfloat16)
        attended_heads.append(attended)
        query_heads.append(query_gradient)
        key_heads.append(grads[0])
        value_heads.append(grads[1])

    return tuple(
        merge_heads(jnp.stack(parts))
        for parts in (attended_heads, query_heads, key_heads, value_heads)
    )


def solution(mesh):
    seq_count = mesh.shape["seq"]
    head_count = mesh.shape["head"]
    pair_mesh = Mesh(
        mesh.devices.reshape(seq_count // 2, 2, head_count), ("sg", "sp", "head")
    )
    tokens = P(None, ("sg", "sp"), "head")
    in_specs = (
        tokens,
        tokens,
        tokens,
        P(None, ("sg", "sp", "head"), None),
        P(None, None, "head", None),
    )
    out_specs = (tokens, tokens, tokens, tokens)
    return jax.shard_map(local, mesh=pair_mesh, in_specs=in_specs, out_specs=out_specs, check_vma=False)
```

```python
import math

import jax
import jax.numpy as jnp
from jax import lax
from jax.sharding import Mesh, PartitionSpec as P


HD = 128


def swap_pair(value):
    return lax.ppermute(value, "sp", [(0, 1), (1, 0)])


def per_head(stored, head_count):
    slices = stored.shape[0]
    rows = stored.shape[1]
    return stored.reshape(slices, rows, head_count, HD).transpose(2, 0, 1, 3)


def merge_heads(split):
    head_count = split.shape[0]
    slices = split.shape[1]
    rows = split.shape[2]
    return split.transpose(1, 2, 0, 3).reshape(slices, rows, head_count * HD)


def layer(queries, keys, values, out_grad, selected):
    groups = lax.axis_size("sg")
    seq_count = 2 * groups
    group_id = lax.axis_index("sg")
    parity = lax.axis_index("sp")
    slices = queries.shape[0]
    half_len = queries.shape[1]
    block_len = 2 * half_len
    head_count = queries.shape[2] // HD
    logit_scale_factor = 1.0 / math.sqrt(HD)
    q_heads = per_head(queries, head_count)
    k_heads = per_head(keys, head_count)
    v_heads = per_head(values, head_count)
    grad_rows = lax.all_to_all(out_grad, "head", split_axis=2, concat_axis=1, tiled=True)
    g_heads = per_head(grad_rows, head_count)
    kv = jnp.stack([k_heads, v_heads])

    sel_g = selected[:, 0::2]
    gid = jnp.arange(groups, dtype=jnp.int32)
    query_block = jnp.stack([gid, seq_count - 1 - gid, seq_count + gid, 2 * seq_count - 1 - gid])
    usable_g = sel_g < query_block[:, :, None, None]
    mine_block = jnp.stack(
        [group_id, seq_count - 1 - group_id, seq_count + group_id, 2 * seq_count - 1 - group_id]
    )
    hits = usable_g[..., None] & (sel_g[..., None] == mine_block)
    need = jnp.any(hits, axis=(0, 3)).astype(jnp.bfloat16)
    mine_sel = lax.dynamic_index_in_dim(sel_g, group_id, 1, keepdims=False)
    mine_usable = mine_sel < mine_block[:, None, None]
    fold = mine_sel % seq_count
    src_group = jnp.where(fold >= groups, seq_count - 1 - fold, fold)
    src_group = jnp.where(mine_usable, src_group, 0)

    send = jnp.einsum(
        "ghf,chfld->gchld", need, kv, preferred_element_type=jnp.float32
    ).astype(jnp.bfloat16)
    held_half = (jnp.arange(slices, dtype=jnp.int32) + parity) % 2
    pairs_kv = kv.reshape(2, head_count, slices // 2, 2, half_len, HD)
    lead = jnp.where(parity == 0, pairs_kv[:, :, :, 0], pairs_kv[:, :, :, 1])
    mate = swap_pair(lead)

    empty_span = jnp.zeros((2, head_count, half_len, HD), jnp.bfloat16)
    own_rows = []
    for slice_id in range(slices):
        second = jnp.concatenate([mate[:, :, slice_id // 2], kv[:, :, slice_id]], axis=2)
        first = jnp.concatenate([kv[:, :, slice_id], empty_span], axis=2)
        own_rows.append(jnp.where(held_half[slice_id] == 1, second, first))
    own_kv = jnp.stack(own_rows, axis=0)

    key_pos = jnp.arange(block_len, dtype=jnp.int32)
    query_pos = held_half[:, None] * half_len + jnp.arange(half_len, dtype=jnp.int32)[None, :]
    own_vis = key_pos[None, None, :] <= query_pos[:, :, None]
    sel_vis = jnp.repeat(mine_usable, block_len, axis=2)
    topk = sel_g.shape[3]

    def attend(operands):
        q_one, k_one, v_one, g_one, vis_one = operands
        attention_logits = (
            jnp.einsum("qd,kd->qk", q_one, k_one, preferred_element_type=jnp.float32)
            * logit_scale_factor
        )
        masked = jnp.where(vis_one, attention_logits, -jnp.inf)
        row_max = jnp.max(masked, axis=-1, keepdims=True)
        exp_vals = jnp.exp(masked - row_max)
        probs = exp_vals / jnp.sum(exp_vals, axis=-1, keepdims=True)
        probability_narrow = probs.astype(jnp.bfloat16)
        attended = jnp.einsum(
            "qk,kd->qd", probability_narrow, v_one, preferred_element_type=jnp.float32
        ).astype(jnp.bfloat16)
        probability_gradient = jnp.einsum(
            "qd,kd->qk", g_one, v_one, preferred_element_type=jnp.float32
        )
        row_delta = jnp.sum(probs * probability_gradient, axis=-1, keepdims=True)
        score_gradient = (probs * (probability_gradient - row_delta)).astype(jnp.bfloat16)
        query_gradient = (
            logit_scale_factor
            * jnp.einsum("qk,kd->qd", score_gradient, k_one, preferred_element_type=jnp.float32)
        ).astype(jnp.bfloat16)
        key_terms = logit_scale_factor * jnp.einsum(
            "qk,qd->kd", score_gradient, q_one, preferred_element_type=jnp.float32
        )
        value_terms = jnp.einsum(
            "qk,qd->kd", probability_narrow, g_one, preferred_element_type=jnp.float32
        )
        return (attended, query_gradient, jnp.stack([key_terms, value_terms]))

    attended_heads = []
    query_heads = []
    got_all = lax.all_to_all(send, "sg", split_axis=0, concat_axis=0, tiled=True)
    outgoing = []
    owned = []
    for head in range(head_count):
        taken = got_all[:, :, head][src_group[:, head]]
        other = swap_pair(taken)
        sel_kv = jnp.stack([taken, other], axis=2)
        sel_kv = sel_kv.transpose(0, 3, 1, 2, 4, 5).reshape(
            slices, 2, 2 * topk * half_len, HD
        )
        every_kv = jnp.concatenate([own_kv[:, :, head], sel_kv], axis=2)
        visible = jnp.concatenate(
            [
                own_vis,
                jnp.broadcast_to(
                    sel_vis[:, head, None, :], (slices, half_len, sel_vis.shape[2])
                ),
            ],
            axis=-1,
        )
        attended, query_gradient, terms = lax.map(
            attend,
            (q_heads[head], every_kv[:, 0], every_kv[:, 1], g_heads[head], visible),
        )
        sel_terms = terms[:, :, block_len:].reshape(slices, 2, topk, 2, half_len, HD)
        mine_terms = sel_terms[:, :, :, 0]
        other_terms = sel_terms[:, :, :, 1].astype(jnp.bfloat16)
        by_pair = terms[:, :, :half_len].reshape(slices // 2, 2, 2, half_len, HD)
        trail = jnp.where(parity == 0, by_pair[:, 1], by_pair[:, 0]).astype(jnp.bfloat16)
        item_count = other_terms.size // (half_len * HD)
        both = jnp.concatenate(
            [other_terms.reshape(item_count, half_len, HD), trail.reshape(-1, half_len, HD)]
        )
        both = swap_pair(both)
        partner_terms = both[:item_count].reshape(other_terms.shape)
        mate_back = both[item_count:].reshape(trail.shape)
        summed = (mine_terms + partner_terms.astype(jnp.float32)).astype(jnp.bfloat16)
        route = (
            (src_group[None, :, head] == gid[:, None, None]) & mine_usable[None, :, head]
        ).astype(jnp.bfloat16)
        send_back = jnp.einsum(
            "gfj,fcjld->gcld", route, summed, preferred_element_type=jnp.float32
        ).astype(jnp.bfloat16)
        outgoing.append(send_back)
        rows_kept = []
        for slice_id in range(slices):
            first = terms[slice_id, :, :half_len] + mate_back[slice_id // 2].astype(jnp.float32)
            second = terms[slice_id, :, half_len:block_len]
            rows_kept.append(jnp.where(held_half[slice_id] == 0, first, second))
        owned.append(jnp.stack(rows_kept, axis=1))
        attended_heads.append(attended)
        query_heads.append(query_gradient)

    back = lax.all_to_all(jnp.stack(outgoing, axis=2), "sg", split_axis=0, concat_axis=0, tiled=True)
    gathered = jnp.einsum("ghf,gchld->chfld", need, back, preferred_element_type=jnp.float32)
    grads = (jnp.stack(owned, axis=1) + gathered).astype(jnp.bfloat16)
    key_heads = grads[0]
    value_heads = grads[1]

    return (
        merge_heads(jnp.stack(attended_heads)),
        merge_heads(jnp.stack(query_heads)),
        merge_heads(key_heads),
        merge_heads(value_heads),
    )


def solution(mesh):
    seq_count = mesh.shape["seq"]
    head_count = mesh.shape["head"]
    pair_mesh = Mesh(
        mesh.devices.reshape(seq_count // 2, 2, head_count), ("sg", "sp", "head")
    )
    tokens = P(None, ("sg", "sp"), "head")
    in_specs = (
        tokens,
        tokens,
        tokens,
        P(None, ("sg", "sp", "head"), None),
        P(None, None, "head", None),
    )
    out_specs = (tokens, tokens, tokens, tokens)
    return jax.shard_map(
        layer, mesh=pair_mesh, in_specs=in_specs, out_specs=out_specs, check_vma=False
    )
```

```python
import math

import jax
import jax.numpy as jnp
from jax import lax
from jax.sharding import Mesh, PartitionSpec as P


HD = 128


def swap_pair(value):
    return lax.ppermute(value, "sp", [(0, 1), (1, 0)])


def per_head(stored, head_count):
    slices = stored.shape[0]
    rows = stored.shape[1]
    return stored.reshape(slices, rows, head_count, HD).transpose(2, 0, 1, 3)


def merge_heads(split):
    head_count = split.shape[0]
    slices = split.shape[1]
    rows = split.shape[2]
    return split.transpose(1, 2, 0, 3).reshape(slices, rows, head_count * HD)


def layer(queries, keys, values, out_grad, selected):
    groups = lax.axis_size("sg")
    seq_count = 2 * groups
    group_id = lax.axis_index("sg")
    parity = lax.axis_index("sp")
    slices = queries.shape[0]
    half_len = queries.shape[1]
    block_len = 2 * half_len
    head_count = queries.shape[2] // HD
    logit_scale_factor = 1.0 / math.sqrt(HD)
    q_heads = per_head(queries, head_count)
    k_heads = per_head(keys, head_count)
    v_heads = per_head(values, head_count)
    grad_rows = lax.all_to_all(out_grad, "head", split_axis=2, concat_axis=1, tiled=True)
    g_heads = per_head(grad_rows, head_count)
    kv = jnp.stack([k_heads, v_heads])

    sel_g = selected[:, 0::2]
    gid = jnp.arange(groups, dtype=jnp.int32)
    query_block = jnp.stack([gid, seq_count - 1 - gid, seq_count + gid, 2 * seq_count - 1 - gid])
    usable_g = sel_g < query_block[:, :, None, None]
    mine_block = jnp.stack(
        [group_id, seq_count - 1 - group_id, seq_count + group_id, 2 * seq_count - 1 - group_id]
    )
    hits = usable_g[..., None] & (sel_g[..., None] == mine_block)
    need = jnp.any(hits, axis=(0, 3)).astype(jnp.bfloat16)
    mine_sel = lax.dynamic_index_in_dim(sel_g, group_id, 1, keepdims=False)
    mine_usable = mine_sel < mine_block[:, None, None]
    fold = mine_sel % seq_count
    src_group = jnp.where(fold >= groups, seq_count - 1 - fold, fold)
    src_group = jnp.where(mine_usable, src_group, 0)

    send = jnp.einsum(
        "ghf,chfld->gchld", need, kv, preferred_element_type=jnp.float32
    ).astype(jnp.bfloat16)
    held_half = (jnp.arange(slices, dtype=jnp.int32) + parity) % 2
    pairs_kv = kv.reshape(2, head_count, slices // 2, 2, half_len, HD)
    lead = jnp.where(parity == 0, pairs_kv[:, :, :, 0], pairs_kv[:, :, :, 1])
    mate = swap_pair(lead)

    empty_span = jnp.zeros((2, head_count, half_len, HD), jnp.bfloat16)
    own_rows = []
    for slice_id in range(slices):
        second = jnp.concatenate([mate[:, :, slice_id // 2], kv[:, :, slice_id]], axis=2)
        first = jnp.concatenate([kv[:, :, slice_id], empty_span], axis=2)
        own_rows.append(jnp.where(held_half[slice_id] == 1, second, first))
    own_kv = jnp.stack(own_rows, axis=0)

    key_pos = jnp.arange(block_len, dtype=jnp.int32)
    query_pos = held_half[:, None] * half_len + jnp.arange(half_len, dtype=jnp.int32)[None, :]
    own_vis = key_pos[None, None, :] <= query_pos[:, :, None]
    sel_vis = jnp.repeat(mine_usable, block_len, axis=2)
    topk = sel_g.shape[3]

    def attend(operands):
        q_one, k_one, v_one, g_one, vis_one = operands
        attention_logits = (
            jnp.einsum("qd,kd->qk", q_one, k_one, preferred_element_type=jnp.float32)
            * logit_scale_factor
        )
        masked = jnp.where(vis_one, attention_logits, -jnp.inf)
        row_max = jnp.max(masked, axis=-1, keepdims=True)
        exp_vals = jnp.exp(masked - row_max)
        probs = exp_vals / jnp.sum(exp_vals, axis=-1, keepdims=True)
        probability_narrow = probs.astype(jnp.bfloat16)
        attended = jnp.einsum(
            "qk,kd->qd", probability_narrow, v_one, preferred_element_type=jnp.float32
        ).astype(jnp.bfloat16)
        probability_gradient = jnp.einsum(
            "qd,kd->qk", g_one, v_one, preferred_element_type=jnp.float32
        )
        row_delta = jnp.sum(probs * probability_gradient, axis=-1, keepdims=True)
        score_gradient = (probs * (probability_gradient - row_delta)).astype(jnp.bfloat16)
        query_gradient = (
            logit_scale_factor
            * jnp.einsum("qk,kd->qd", score_gradient, k_one, preferred_element_type=jnp.float32)
        ).astype(jnp.bfloat16)
        key_terms = logit_scale_factor * jnp.einsum(
            "qk,qd->kd", score_gradient, q_one, preferred_element_type=jnp.float32
        )
        value_terms = jnp.einsum(
            "qk,qd->kd", probability_narrow, g_one, preferred_element_type=jnp.float32
        )
        return (attended, query_gradient, jnp.stack([key_terms, value_terms]))

    attended_heads = []
    query_heads = []
    key_heads = []
    value_heads = []
    for head in range(head_count):
        got = lax.all_to_all(send[:, :, head], "sg", split_axis=0, concat_axis=0, tiled=True)
        taken = got[src_group[:, head]]
        other = swap_pair(taken)
        sel_kv = jnp.stack([taken, other], axis=2)
        sel_kv = sel_kv.transpose(0, 3, 1, 2, 4, 5).reshape(
            slices, 2, 2 * topk * half_len, HD
        )
        every_kv = jnp.concatenate([own_kv[:, :, head], sel_kv], axis=2)
        visible = jnp.concatenate(
            [
                own_vis,
                jnp.broadcast_to(
                    sel_vis[:, head, None, :], (slices, half_len, sel_vis.shape[2])
                ),
            ],
            axis=-1,
        )
        attended, query_gradient, terms = lax.map(
            attend,
            (q_heads[head], every_kv[:, 0], every_kv[:, 1], g_heads[head], visible),
        )
        sel_terms = terms[:, :, block_len:].reshape(slices, 2, topk, 2, half_len, HD)
        mine_terms = sel_terms[:, :, :, 0]
        other_terms = sel_terms[:, :, :, 1].astype(jnp.bfloat16)
        by_pair = terms[:, :, :half_len].reshape(slices // 2, 2, 2, half_len, HD)
        trail = jnp.where(parity == 0, by_pair[:, 1], by_pair[:, 0]).astype(jnp.bfloat16)
        item_count = other_terms.size // (half_len * HD)
        both = jnp.concatenate(
            [other_terms.reshape(item_count, half_len, HD), trail.reshape(-1, half_len, HD)]
        )
        both = swap_pair(both)
        partner_terms = both[:item_count].reshape(other_terms.shape)
        mate_back = both[item_count:].reshape(trail.shape)
        summed = (mine_terms + partner_terms.astype(jnp.float32)).astype(jnp.bfloat16)
        route = (
            (src_group[None, :, head] == gid[:, None, None]) & mine_usable[None, :, head]
        ).astype(jnp.bfloat16)
        send_back = jnp.einsum(
            "gfj,fcjld->gcld", route, summed, preferred_element_type=jnp.float32
        ).astype(jnp.bfloat16)
        back = lax.all_to_all(send_back, "sg", split_axis=0, concat_axis=0, tiled=True)
        gathered = jnp.einsum(
            "gf,gcld->cfld", need[:, head], back, preferred_element_type=jnp.float32
        )
        rows_kept = []
        for slice_id in range(slices):
            first = terms[slice_id, :, :half_len] + mate_back[slice_id // 2].astype(jnp.float32)
            second = terms[slice_id, :, half_len:block_len]
            rows_kept.append(jnp.where(held_half[slice_id] == 0, first, second))
        grads = (jnp.stack(rows_kept, axis=1) + gathered).astype(jnp.bfloat16)
        attended_heads.append(attended)
        query_heads.append(query_gradient)
        key_heads.append(grads[0])
        value_heads.append(grads[1])

    return tuple(
        merge_heads(jnp.stack(parts))
        for parts in (attended_heads, query_heads, key_heads, value_heads)
    )


def solution(mesh):
    seq_count = mesh.shape["seq"]
    head_count = mesh.shape["head"]
    pair_mesh = Mesh(
        mesh.devices.reshape(seq_count // 2, 2, head_count), ("sg", "sp", "head")
    )
    tokens = P(None, ("sg", "sp"), "head")
    in_specs = (
        tokens,
        tokens,
        tokens,
        P(None, ("sg", "sp", "head"), None),
        P(None, None, "head", None),
    )
    out_specs = (tokens, tokens, tokens, tokens)
    return jax.shard_map(
        layer, mesh=pair_mesh, in_specs=in_specs, out_specs=out_specs, check_vma=False
    )
```

```python
import math

import jax
import jax.numpy as jnp
from jax import lax
from jax.sharding import Mesh, PartitionSpec as P


HD = 128


def swap_pair(value):
    return lax.ppermute(value, "sp", [(0, 1), (1, 0)])


def per_head(stored, head_count):
    slices = stored.shape[0]
    rows = stored.shape[1]
    return stored.reshape(slices, rows, head_count, HD).transpose(2, 0, 1, 3)


def merge_heads(split):
    head_count = split.shape[0]
    slices = split.shape[1]
    rows = split.shape[2]
    return split.transpose(1, 2, 0, 3).reshape(slices, rows, head_count * HD)


def layer(queries, keys, values, out_grad, selected):
    groups = lax.axis_size("sg")
    seq_count = 2 * groups
    group_id = lax.axis_index("sg")
    parity = lax.axis_index("sp")
    slices = queries.shape[0]
    half_len = queries.shape[1]
    block_len = 2 * half_len
    head_count = queries.shape[2] // HD
    logit_scale_factor = 1.0 / math.sqrt(HD)
    q_heads = per_head(queries, head_count)
    k_heads = per_head(keys, head_count)
    v_heads = per_head(values, head_count)
    grad_rows = lax.all_to_all(out_grad, "head", split_axis=2, concat_axis=1, tiled=True)
    g_heads = per_head(grad_rows, head_count)
    kv = jnp.stack([k_heads, v_heads])

    sel_g = selected[:, 0::2]
    gid = jnp.arange(groups, dtype=jnp.int32)
    query_block = jnp.stack([gid, seq_count - 1 - gid, seq_count + gid, 2 * seq_count - 1 - gid])
    usable_g = sel_g < query_block[:, :, None, None]
    mine_block = jnp.stack(
        [group_id, seq_count - 1 - group_id, seq_count + group_id, 2 * seq_count - 1 - group_id]
    )
    hits = usable_g[..., None] & (sel_g[..., None] == mine_block)
    need = jnp.any(hits, axis=(0, 3)).astype(jnp.bfloat16)
    mine_sel = lax.dynamic_index_in_dim(sel_g, group_id, 1, keepdims=False)
    mine_usable = mine_sel < mine_block[:, None, None]
    fold = mine_sel % seq_count
    src_group = jnp.where(fold >= groups, seq_count - 1 - fold, fold)
    src_group = jnp.where(mine_usable, src_group, 0)

    send = jnp.einsum(
        "ghf,chfld->gchld", need, kv, preferred_element_type=jnp.float32
    ).astype(jnp.bfloat16)
    held_half = (jnp.arange(slices, dtype=jnp.int32) + parity) % 2
    pairs_kv = kv.reshape(2, head_count, slices // 2, 2, half_len, HD)
    lead = jnp.where(parity == 0, pairs_kv[:, :, :, 0], pairs_kv[:, :, :, 1])
    mate = swap_pair(lead)

    empty_span = jnp.zeros((2, head_count, half_len, HD), jnp.bfloat16)
    own_rows = []
    for slice_id in range(slices):
        second = jnp.concatenate([mate[:, :, slice_id // 2], kv[:, :, slice_id]], axis=2)
        first = jnp.concatenate([kv[:, :, slice_id], empty_span], axis=2)
        own_rows.append(jnp.where(held_half[slice_id] == 1, second, first))
    own_kv = jnp.stack(own_rows, axis=0)

    key_pos = jnp.arange(block_len, dtype=jnp.int32)
    query_pos = held_half[:, None] * half_len + jnp.arange(half_len, dtype=jnp.int32)[None, :]
    own_vis = key_pos[None, None, :] <= query_pos[:, :, None]
    sel_vis = jnp.repeat(mine_usable, block_len, axis=2)
    topk = sel_g.shape[3]

    def attend(operands):
        q_one, k_one, v_one, g_one, vis_one = operands
        attention_logits = (
            jnp.einsum("qd,kd->qk", q_one, k_one, preferred_element_type=jnp.float32)
            * logit_scale_factor
        )
        masked = jnp.where(vis_one, attention_logits, -jnp.inf)
        row_max = jnp.max(masked, axis=-1, keepdims=True)
        exp_vals = jnp.exp(masked - row_max)
        probs = exp_vals / jnp.sum(exp_vals, axis=-1, keepdims=True)
        probability_narrow = probs.astype(jnp.bfloat16)
        attended = jnp.einsum(
            "qk,kd->qd", probability_narrow, v_one, preferred_element_type=jnp.float32
        ).astype(jnp.bfloat16)
        probability_gradient = jnp.einsum(
            "qd,kd->qk", g_one, v_one, preferred_element_type=jnp.float32
        )
        row_delta = jnp.sum(probs * probability_gradient, axis=-1, keepdims=True)
        score_gradient = (probs * (probability_gradient - row_delta)).astype(jnp.bfloat16)
        query_gradient = (
            logit_scale_factor
            * jnp.einsum("qk,kd->qd", score_gradient, k_one, preferred_element_type=jnp.float32)
        ).astype(jnp.bfloat16)
        key_terms = logit_scale_factor * jnp.einsum(
            "qk,qd->kd", score_gradient, q_one, preferred_element_type=jnp.float32
        )
        value_terms = jnp.einsum(
            "qk,qd->kd", probability_narrow, g_one, preferred_element_type=jnp.float32
        )
        return (attended, query_gradient, jnp.stack([key_terms, value_terms]))

    attended_heads = []
    query_heads = []
    outgoing = []
    owned = []
    for head in range(head_count):
        got = lax.all_to_all(send[:, :, head], "sg", split_axis=0, concat_axis=0, tiled=True)
        taken = got[src_group[:, head]]
        other = swap_pair(taken)
        sel_kv = jnp.stack([taken, other], axis=2)
        sel_kv = sel_kv.transpose(0, 3, 1, 2, 4, 5).reshape(
            slices, 2, 2 * topk * half_len, HD
        )
        every_kv = jnp.concatenate([own_kv[:, :, head], sel_kv], axis=2)
        visible = jnp.concatenate(
            [
                own_vis,
                jnp.broadcast_to(
                    sel_vis[:, head, None, :], (slices, half_len, sel_vis.shape[2])
                ),
            ],
            axis=-1,
        )
        attended, query_gradient, terms = lax.map(
            attend,
            (q_heads[head], every_kv[:, 0], every_kv[:, 1], g_heads[head], visible),
        )
        sel_terms = terms[:, :, block_len:].reshape(slices, 2, topk, 2, half_len, HD)
        mine_terms = sel_terms[:, :, :, 0]
        other_terms = sel_terms[:, :, :, 1].astype(jnp.bfloat16)
        by_pair = terms[:, :, :half_len].reshape(slices // 2, 2, 2, half_len, HD)
        trail = jnp.where(parity == 0, by_pair[:, 1], by_pair[:, 0]).astype(jnp.bfloat16)
        item_count = other_terms.size // (half_len * HD)
        both = jnp.concatenate(
            [other_terms.reshape(item_count, half_len, HD), trail.reshape(-1, half_len, HD)]
        )
        both = swap_pair(both)
        partner_terms = both[:item_count].reshape(other_terms.shape)
        mate_back = both[item_count:].reshape(trail.shape)
        summed = (mine_terms + partner_terms.astype(jnp.float32)).astype(jnp.bfloat16)
        route = (
            (src_group[None, :, head] == gid[:, None, None]) & mine_usable[None, :, head]
        ).astype(jnp.bfloat16)
        send_back = jnp.einsum(
            "gfj,fcjld->gcld", route, summed, preferred_element_type=jnp.float32
        ).astype(jnp.bfloat16)
        outgoing.append(send_back)
        rows_kept = []
        for slice_id in range(slices):
            first = terms[slice_id, :, :half_len] + mate_back[slice_id // 2].astype(jnp.float32)
            second = terms[slice_id, :, half_len:block_len]
            rows_kept.append(jnp.where(held_half[slice_id] == 0, first, second))
        owned.append(jnp.stack(rows_kept, axis=1))
        attended_heads.append(attended)
        query_heads.append(query_gradient)

    back = lax.all_to_all(jnp.stack(outgoing, axis=2), "sg", split_axis=0, concat_axis=0, tiled=True)
    gathered = jnp.einsum("ghf,gchld->chfld", need, back, preferred_element_type=jnp.float32)
    grads = (jnp.stack(owned, axis=1) + gathered).astype(jnp.bfloat16)
    return (
        merge_heads(jnp.stack(attended_heads)),
        merge_heads(jnp.stack(query_heads)),
        merge_heads(grads[0]),
        merge_heads(grads[1]),
    )


def solution(mesh):
    seq_count = mesh.shape["seq"]
    head_count = mesh.shape["head"]
    pair_mesh = Mesh(
        mesh.devices.reshape(seq_count // 2, 2, head_count), ("sg", "sp", "head")
    )
    tokens = P(None, ("sg", "sp"), "head")
    in_specs = (
        tokens,
        tokens,
        tokens,
        P(None, ("sg", "sp", "head"), None),
        P(None, None, "head", None),
    )
    out_specs = (tokens, tokens, tokens, tokens)
    return jax.shard_map(
        layer, mesh=pair_mesh, in_specs=in_specs, out_specs=out_specs, check_vma=False
    )
```

```python
import math

import jax
import jax.numpy as jnp
from jax import lax
from jax.sharding import Mesh, PartitionSpec as P


HD = 128


def swap_pair(value):
    return lax.ppermute(value, "sp", [(0, 1), (1, 0)])


def per_head(stored, head_count):
    slices = stored.shape[0]
    rows = stored.shape[1]
    return stored.reshape(slices, rows, head_count, HD).transpose(2, 0, 1, 3)


def merge_heads(split):
    head_count = split.shape[0]
    slices = split.shape[1]
    rows = split.shape[2]
    return split.transpose(1, 2, 0, 3).reshape(slices, rows, head_count * HD)


def layer(queries, keys, values, out_grad, selected):
    groups = lax.axis_size("sg")
    seq_count = 2 * groups
    group_id = lax.axis_index("sg")
    parity = lax.axis_index("sp")
    slices = queries.shape[0]
    half_len = queries.shape[1]
    block_len = 2 * half_len
    head_count = queries.shape[2] // HD
    logit_scale_factor = 1.0 / math.sqrt(HD)
    q_heads = per_head(queries, head_count)
    k_heads = per_head(keys, head_count)
    v_heads = per_head(values, head_count)
    grad_rows = lax.all_to_all(out_grad, "head", split_axis=2, concat_axis=1, tiled=True)
    g_heads = per_head(grad_rows, head_count)
    kv = jnp.stack([k_heads, v_heads])

    sel_g = selected[:, 0::2]
    gid = jnp.arange(groups, dtype=jnp.int32)
    query_block = jnp.stack([gid, seq_count - 1 - gid, seq_count + gid, 2 * seq_count - 1 - gid])
    usable_g = sel_g < query_block[:, :, None, None]
    mine_block = jnp.stack(
        [group_id, seq_count - 1 - group_id, seq_count + group_id, 2 * seq_count - 1 - group_id]
    )
    hits = usable_g[..., None] & (sel_g[..., None] == mine_block)
    need = jnp.any(hits, axis=(0, 3)).astype(jnp.bfloat16)
    mine_sel = lax.dynamic_index_in_dim(sel_g, group_id, 1, keepdims=False)
    mine_usable = mine_sel < mine_block[:, None, None]
    fold = mine_sel % seq_count
    src_group = jnp.where(fold >= groups, seq_count - 1 - fold, fold)
    src_group = jnp.where(mine_usable, src_group, 0)

    send = jnp.einsum(
        "ghf,chfld->gchld", need, kv, preferred_element_type=jnp.float32
    ).astype(jnp.bfloat16)
    held_half = (jnp.arange(slices, dtype=jnp.int32) + parity) % 2
    pairs_kv = kv.reshape(2, head_count, slices // 2, 2, half_len, HD)
    lead = jnp.where(parity == 0, pairs_kv[:, :, :, 0], pairs_kv[:, :, :, 1])

    def own_keys(mate):

        empty_span = jnp.zeros((2, head_count, half_len, HD), jnp.bfloat16)
        own_rows = []
        for slice_id in range(slices):
            second = jnp.concatenate([mate[:, :, slice_id // 2], kv[:, :, slice_id]], axis=2)
            first = jnp.concatenate([kv[:, :, slice_id], empty_span], axis=2)
            own_rows.append(jnp.where(held_half[slice_id] == 1, second, first))
        own_kv = jnp.stack(own_rows, axis=0)
        return own_kv

    key_pos = jnp.arange(block_len, dtype=jnp.int32)
    query_pos = held_half[:, None] * half_len + jnp.arange(half_len, dtype=jnp.int32)[None, :]
    own_vis = key_pos[None, None, :] <= query_pos[:, :, None]
    sel_vis = jnp.repeat(mine_usable, block_len, axis=2)
    topk = sel_g.shape[3]

    def attend(operands):
        q_one, k_one, v_one, g_one, vis_one = operands
        attention_logits = (
            jnp.einsum("qd,kd->qk", q_one, k_one, preferred_element_type=jnp.float32)
            * logit_scale_factor
        )
        masked = jnp.where(vis_one, attention_logits, -jnp.inf)
        row_max = jnp.max(masked, axis=-1, keepdims=True)
        exp_vals = jnp.exp(masked - row_max)
        probs = exp_vals / jnp.sum(exp_vals, axis=-1, keepdims=True)
        probability_narrow = probs.astype(jnp.bfloat16)
        attended = jnp.einsum(
            "qk,kd->qd", probability_narrow, v_one, preferred_element_type=jnp.float32
        ).astype(jnp.bfloat16)
        probability_gradient = jnp.einsum(
            "qd,kd->qk", g_one, v_one, preferred_element_type=jnp.float32
        )
        row_delta = jnp.sum(probs * probability_gradient, axis=-1, keepdims=True)
        score_gradient = (probs * (probability_gradient - row_delta)).astype(jnp.bfloat16)
        query_gradient = (
            logit_scale_factor
            * jnp.einsum("qk,kd->qd", score_gradient, k_one, preferred_element_type=jnp.float32)
        ).astype(jnp.bfloat16)
        key_terms = logit_scale_factor * jnp.einsum(
            "qk,qd->kd", score_gradient, q_one, preferred_element_type=jnp.float32
        )
        value_terms = jnp.einsum(
            "qk,qd->kd", probability_narrow, g_one, preferred_element_type=jnp.float32
        )
        return (attended, query_gradient, jnp.stack([key_terms, value_terms]))

    attended_heads = []
    query_heads = []
    outgoing = []
    owned = []
    for head in range(head_count):
        got = lax.all_to_all(send[:, :, head], "sg", split_axis=0, concat_axis=0, tiled=True)
        taken = got[src_group[:, head]]
        if head == 0:
            span_count = taken.size // (half_len * HD)
            sent = jnp.concatenate(
                [taken.reshape(span_count, half_len, HD), lead.reshape(-1, half_len, HD)]
            )
            sent = swap_pair(sent)
            other = sent[:span_count].reshape(taken.shape)
            own_kv = own_keys(sent[span_count:].reshape(lead.shape))
        else:
            other = swap_pair(taken)
        sel_kv = jnp.stack([taken, other], axis=2)
        sel_kv = sel_kv.transpose(0, 3, 1, 2, 4, 5).reshape(
            slices, 2, 2 * topk * half_len, HD
        )
        every_kv = jnp.concatenate([own_kv[:, :, head], sel_kv], axis=2)
        visible = jnp.concatenate(
            [
                own_vis,
                jnp.broadcast_to(
                    sel_vis[:, head, None, :], (slices, half_len, sel_vis.shape[2])
                ),
            ],
            axis=-1,
        )
        attended, query_gradient, terms = lax.map(
            attend,
            (q_heads[head], every_kv[:, 0], every_kv[:, 1], g_heads[head], visible),
        )
        sel_terms = terms[:, :, block_len:].reshape(slices, 2, topk, 2, half_len, HD)
        mine_terms = sel_terms[:, :, :, 0]
        other_terms = sel_terms[:, :, :, 1].astype(jnp.bfloat16)
        by_pair = terms[:, :, :half_len].reshape(slices // 2, 2, 2, half_len, HD)
        trail = jnp.where(parity == 0, by_pair[:, 1], by_pair[:, 0]).astype(jnp.bfloat16)
        item_count = other_terms.size // (half_len * HD)
        both = jnp.concatenate(
            [other_terms.reshape(item_count, half_len, HD), trail.reshape(-1, half_len, HD)]
        )
        both = swap_pair(both)
        partner_terms = both[:item_count].reshape(other_terms.shape)
        mate_back = both[item_count:].reshape(trail.shape)
        summed = (mine_terms + partner_terms.astype(jnp.float32)).astype(jnp.bfloat16)
        route = (
            (src_group[None, :, head] == gid[:, None, None]) & mine_usable[None, :, head]
        ).astype(jnp.bfloat16)
        send_back = jnp.einsum(
            "gfj,fcjld->gcld", route, summed, preferred_element_type=jnp.float32
        ).astype(jnp.bfloat16)
        outgoing.append(send_back)
        rows_kept = []
        for slice_id in range(slices):
            first = terms[slice_id, :, :half_len] + mate_back[slice_id // 2].astype(jnp.float32)
            second = terms[slice_id, :, half_len:block_len]
            rows_kept.append(jnp.where(held_half[slice_id] == 0, first, second))
        owned.append(jnp.stack(rows_kept, axis=1))
        attended_heads.append(attended)
        query_heads.append(query_gradient)

    back = lax.all_to_all(jnp.stack(outgoing, axis=2), "sg", split_axis=0, concat_axis=0, tiled=True)
    gathered = jnp.einsum("ghf,gchld->chfld", need, back, preferred_element_type=jnp.float32)
    grads = (jnp.stack(owned, axis=1) + gathered).astype(jnp.bfloat16)
    return (
        merge_heads(jnp.stack(attended_heads)),
        merge_heads(jnp.stack(query_heads)),
        merge_heads(grads[0]),
        merge_heads(grads[1]),
    )


def solution(mesh):
    seq_count = mesh.shape["seq"]
    head_count = mesh.shape["head"]
    pair_mesh = Mesh(
        mesh.devices.reshape(seq_count // 2, 2, head_count), ("sg", "sp", "head")
    )
    tokens = P(None, ("sg", "sp"), "head")
    in_specs = (
        tokens,
        tokens,
        tokens,
        P(None, ("sg", "sp", "head"), None),
        P(None, None, "head", None),
    )
    out_specs = (tokens, tokens, tokens, tokens)
    return jax.shard_map(
        layer, mesh=pair_mesh, in_specs=in_specs, out_specs=out_specs, check_vma=False
    )
```

```python
import math

import jax
import jax.numpy as jnp
from jax import lax
from jax.sharding import Mesh, PartitionSpec as P


HD = 128


def swap_pair(value):
    return lax.ppermute(value, "sp", [(0, 1), (1, 0)])


def per_head(stored, head_count):
    slices = stored.shape[0]
    rows = stored.shape[1]
    return stored.reshape(slices, rows, head_count, HD).transpose(2, 0, 1, 3)


def merge_heads(split):
    head_count = split.shape[0]
    slices = split.shape[1]
    rows = split.shape[2]
    return split.transpose(1, 2, 0, 3).reshape(slices, rows, head_count * HD)


def layer(queries, keys, values, out_grad, selected):
    groups = lax.axis_size("sg")
    seq_count = 2 * groups
    group_id = lax.axis_index("sg")
    parity = lax.axis_index("sp")
    slices = queries.shape[0]
    half_len = queries.shape[1]
    block_len = 2 * half_len
    head_count = queries.shape[2] // HD
    logit_scale_factor = 1.0 / math.sqrt(HD)
    q_heads = per_head(queries, head_count)
    k_heads = per_head(keys, head_count)
    v_heads = per_head(values, head_count)
    grad_rows = lax.all_to_all(out_grad, "head", split_axis=2, concat_axis=1, tiled=True)
    g_heads = per_head(grad_rows, head_count)
    kv = jnp.stack([k_heads, v_heads])

    sel_g = selected[:, 0::2]
    gid = jnp.arange(groups, dtype=jnp.int32)
    query_block = jnp.stack([gid, seq_count - 1 - gid, seq_count + gid, 2 * seq_count - 1 - gid])
    usable_g = sel_g < query_block[:, :, None, None]
    mine_block = jnp.stack(
        [group_id, seq_count - 1 - group_id, seq_count + group_id, 2 * seq_count - 1 - group_id]
    )
    hits = usable_g[..., None] & (sel_g[..., None] == mine_block)
    need = jnp.any(hits, axis=(0, 3)).astype(jnp.bfloat16)
    mine_sel = lax.dynamic_index_in_dim(sel_g, group_id, 1, keepdims=False)
    mine_usable = mine_sel < mine_block[:, None, None]
    fold = mine_sel % seq_count
    src_group = jnp.where(fold >= groups, seq_count - 1 - fold, fold)
    src_group = jnp.where(mine_usable, src_group, 0)

    held_half = (jnp.arange(slices, dtype=jnp.int32) + parity) % 2
    pairs_kv = kv.reshape(2, head_count, slices // 2, 2, half_len, HD)
    lead = jnp.where(parity == 0, pairs_kv[:, :, :, 0], pairs_kv[:, :, :, 1])
    mate = swap_pair(lead)

    empty_span = jnp.zeros((2, head_count, half_len, HD), jnp.bfloat16)
    own_rows = []
    for slice_id in range(slices):
        second = jnp.concatenate([mate[:, :, slice_id // 2], kv[:, :, slice_id]], axis=2)
        first = jnp.concatenate([kv[:, :, slice_id], empty_span], axis=2)
        own_rows.append(jnp.where(held_half[slice_id] == 1, second, first))
    own_kv = jnp.stack(own_rows, axis=0)

    key_pos = jnp.arange(block_len, dtype=jnp.int32)
    query_pos = held_half[:, None] * half_len + jnp.arange(half_len, dtype=jnp.int32)[None, :]
    own_vis = key_pos[None, None, :] <= query_pos[:, :, None]
    sel_vis = jnp.repeat(mine_usable, block_len, axis=2)
    topk = sel_g.shape[3]

    def attend(operands):
        q_one, k_one, v_one, g_one, vis_one = operands
        attention_logits = (
            jnp.einsum("qd,kd->qk", q_one, k_one, preferred_element_type=jnp.float32)
            * logit_scale_factor
        )
        masked = jnp.where(vis_one, attention_logits, -jnp.inf)
        row_max = jnp.max(masked, axis=-1, keepdims=True)
        exp_vals = jnp.exp(masked - row_max)
        probs = exp_vals / jnp.sum(exp_vals, axis=-1, keepdims=True)
        probability_narrow = probs.astype(jnp.bfloat16)
        attended = jnp.einsum(
            "qk,kd->qd", probability_narrow, v_one, preferred_element_type=jnp.float32
        ).astype(jnp.bfloat16)
        probability_gradient = jnp.einsum(
            "qd,kd->qk", g_one, v_one, preferred_element_type=jnp.float32
        )
        row_delta = jnp.sum(probs * probability_gradient, axis=-1, keepdims=True)
        score_gradient = (probs * (probability_gradient - row_delta)).astype(jnp.bfloat16)
        query_gradient = (
            logit_scale_factor
            * jnp.einsum("qk,kd->qd", score_gradient, k_one, preferred_element_type=jnp.float32)
        ).astype(jnp.bfloat16)
        key_terms = logit_scale_factor * jnp.einsum(
            "qk,qd->kd", score_gradient, q_one, preferred_element_type=jnp.float32
        )
        value_terms = jnp.einsum(
            "qk,qd->kd", probability_narrow, g_one, preferred_element_type=jnp.float32
        )
        return (attended, query_gradient, jnp.stack([key_terms, value_terms]))

    attended_heads = []
    query_heads = []
    outgoing = []
    owned = []
    for head in range(head_count):
        send_head = jnp.einsum(
            "gf,cfld->gcld", need[:, head], kv[:, head], preferred_element_type=jnp.float32
        ).astype(jnp.bfloat16)
        got = lax.all_to_all(send_head, "sg", split_axis=0, concat_axis=0, tiled=True)
        taken = got[src_group[:, head]]
        other = swap_pair(taken)
        sel_kv = jnp.stack([taken, other], axis=2)
        sel_kv = sel_kv.transpose(0, 3, 1, 2, 4, 5).reshape(
            slices, 2, 2 * topk * half_len, HD
        )
        every_kv = jnp.concatenate([own_kv[:, :, head], sel_kv], axis=2)
        visible = jnp.concatenate(
            [
                own_vis,
                jnp.broadcast_to(
                    sel_vis[:, head, None, :], (slices, half_len, sel_vis.shape[2])
                ),
            ],
            axis=-1,
        )
        attended, query_gradient, terms = lax.map(
            attend,
            (q_heads[head], every_kv[:, 0], every_kv[:, 1], g_heads[head], visible),
        )
        sel_terms = terms[:, :, block_len:].reshape(slices, 2, topk, 2, half_len, HD)
        mine_terms = sel_terms[:, :, :, 0]
        other_terms = sel_terms[:, :, :, 1].astype(jnp.bfloat16)
        by_pair = terms[:, :, :half_len].reshape(slices // 2, 2, 2, half_len, HD)
        trail = jnp.where(parity == 0, by_pair[:, 1], by_pair[:, 0]).astype(jnp.bfloat16)
        item_count = other_terms.size // (half_len * HD)
        both = jnp.concatenate(
            [other_terms.reshape(item_count, half_len, HD), trail.reshape(-1, half_len, HD)]
        )
        both = swap_pair(both)
        partner_terms = both[:item_count].reshape(other_terms.shape)
        mate_back = both[item_count:].reshape(trail.shape)
        summed = (mine_terms + partner_terms.astype(jnp.float32)).astype(jnp.bfloat16)
        route = (
            (src_group[None, :, head] == gid[:, None, None]) & mine_usable[None, :, head]
        ).astype(jnp.bfloat16)
        send_back = jnp.einsum(
            "gfj,fcjld->gcld", route, summed, preferred_element_type=jnp.float32
        ).astype(jnp.bfloat16)
        outgoing.append(send_back)
        rows_kept = []
        for slice_id in range(slices):
            first = terms[slice_id, :, :half_len] + mate_back[slice_id // 2].astype(jnp.float32)
            second = terms[slice_id, :, half_len:block_len]
            rows_kept.append(jnp.where(held_half[slice_id] == 0, first, second))
        owned.append(jnp.stack(rows_kept, axis=1))
        attended_heads.append(attended)
        query_heads.append(query_gradient)

    back = lax.all_to_all(jnp.stack(outgoing, axis=2), "sg", split_axis=0, concat_axis=0, tiled=True)
    gathered = jnp.einsum("ghf,gchld->chfld", need, back, preferred_element_type=jnp.float32)
    grads = (jnp.stack(owned, axis=1) + gathered).astype(jnp.bfloat16)
    return (
        merge_heads(jnp.stack(attended_heads)),
        merge_heads(jnp.stack(query_heads)),
        merge_heads(grads[0]),
        merge_heads(grads[1]),
    )


def solution(mesh):
    seq_count = mesh.shape["seq"]
    head_count = mesh.shape["head"]
    pair_mesh = Mesh(
        mesh.devices.reshape(seq_count // 2, 2, head_count), ("sg", "sp", "head")
    )
    tokens = P(None, ("sg", "sp"), "head")
    in_specs = (
        tokens,
        tokens,
        tokens,
        P(None, ("sg", "sp", "head"), None),
        P(None, None, "head", None),
    )
    out_specs = (tokens, tokens, tokens, tokens)
    return jax.shard_map(
        layer, mesh=pair_mesh, in_specs=in_specs, out_specs=out_specs, check_vma=False
    )
```

```python
import math

import jax
import jax.numpy as jnp
from jax import lax
from jax.sharding import Mesh, PartitionSpec as P


HD = 128


def swap_pair(value):
    return lax.ppermute(value, "sp", [(0, 1), (1, 0)])


def per_head(stored, head_count):
    slices = stored.shape[0]
    rows = stored.shape[1]
    return stored.reshape(slices, rows, head_count, HD).transpose(2, 0, 1, 3)


def merge_heads(split):
    head_count = split.shape[0]
    slices = split.shape[1]
    rows = split.shape[2]
    return split.transpose(1, 2, 0, 3).reshape(slices, rows, head_count * HD)


def layer(queries, keys, values, out_grad, selected):
    groups = lax.axis_size("sg")
    seq_count = 2 * groups
    group_id = lax.axis_index("sg")
    parity = lax.axis_index("sp")
    slices = queries.shape[0]
    half_len = queries.shape[1]
    block_len = 2 * half_len
    head_count = queries.shape[2] // HD
    logit_scale_factor = 1.0 / math.sqrt(HD)
    q_heads = per_head(queries, head_count)
    k_heads = per_head(keys, head_count)
    v_heads = per_head(values, head_count)
    grad_rows = lax.all_to_all(out_grad, "head", split_axis=2, concat_axis=1, tiled=True)
    g_heads = per_head(grad_rows, head_count)
    kv = jnp.stack([k_heads, v_heads])

    sel_g = selected[:, 0::2]
    gid = jnp.arange(groups, dtype=jnp.int32)
    query_block = jnp.stack([gid, seq_count - 1 - gid, seq_count + gid, 2 * seq_count - 1 - gid])
    usable_g = sel_g < query_block[:, :, None, None]
    mine_block = jnp.stack(
        [group_id, seq_count - 1 - group_id, seq_count + group_id, 2 * seq_count - 1 - group_id]
    )
    hits = usable_g[..., None] & (sel_g[..., None] == mine_block)
    need = jnp.any(hits, axis=(0, 3)).astype(jnp.bfloat16)
    mine_sel = lax.dynamic_index_in_dim(sel_g, group_id, 1, keepdims=False)
    mine_usable = mine_sel < mine_block[:, None, None]
    fold = mine_sel % seq_count
    src_group = jnp.where(fold >= groups, seq_count - 1 - fold, fold)
    src_group = jnp.where(mine_usable, src_group, 0)

    held_half = (jnp.arange(slices, dtype=jnp.int32) + parity) % 2
    pairs_kv = kv.reshape(2, head_count, slices // 2, 2, half_len, HD)
    lead = jnp.where(parity == 0, pairs_kv[:, :, :, 0], pairs_kv[:, :, :, 1])
    mate = swap_pair(lead)

    empty_span = jnp.zeros((2, head_count, half_len, HD), jnp.bfloat16)
    own_rows = []
    for slice_id in range(slices):
        second = jnp.concatenate([mate[:, :, slice_id // 2], kv[:, :, slice_id]], axis=2)
        first = jnp.concatenate([kv[:, :, slice_id], empty_span], axis=2)
        own_rows.append(jnp.where(held_half[slice_id] == 1, second, first))
    own_kv = jnp.stack(own_rows, axis=0)

    key_pos = jnp.arange(block_len, dtype=jnp.int32)
    query_pos = held_half[:, None] * half_len + jnp.arange(half_len, dtype=jnp.int32)[None, :]
    own_vis = key_pos[None, None, :] <= query_pos[:, :, None]
    sel_vis = jnp.repeat(mine_usable, block_len, axis=2)
    topk = sel_g.shape[3]

    def attend(operands):
        q_one, k_one, v_one, g_one, vis_one = operands
        attention_logits = (
            jnp.einsum("qd,kd->qk", q_one, k_one, preferred_element_type=jnp.float32)
            * logit_scale_factor
        )
        masked = jnp.where(vis_one, attention_logits, -jnp.inf)
        row_max = jnp.max(masked, axis=-1, keepdims=True)
        exp_vals = jnp.exp(masked - row_max)
        probs = exp_vals / jnp.sum(exp_vals, axis=-1, keepdims=True)
        probability_narrow = probs.astype(jnp.bfloat16)
        attended = jnp.einsum(
            "qk,kd->qd", probability_narrow, v_one, preferred_element_type=jnp.float32
        ).astype(jnp.bfloat16)
        probability_gradient = jnp.einsum(
            "qd,kd->qk", g_one, v_one, preferred_element_type=jnp.float32
        )
        row_delta = jnp.sum(probs * probability_gradient, axis=-1, keepdims=True)
        score_gradient = (probs * (probability_gradient - row_delta)).astype(jnp.bfloat16)
        query_gradient = (
            logit_scale_factor
            * jnp.einsum("qk,kd->qd", score_gradient, k_one, preferred_element_type=jnp.float32)
        ).astype(jnp.bfloat16)
        key_terms = logit_scale_factor * jnp.einsum(
            "qk,qd->kd", score_gradient, q_one, preferred_element_type=jnp.float32
        )
        value_terms = jnp.einsum(
            "qk,qd->kd", probability_narrow, g_one, preferred_element_type=jnp.float32
        )
        return (attended, query_gradient, jnp.stack([key_terms, value_terms]))

    attended_heads = []
    query_heads = []
    outgoing = []
    owned = []
    for head in range(head_count):
        send_head = jnp.einsum(
            "gf,cfld->gcld", need[:, head], kv[:, head], preferred_element_type=jnp.float32
        ).astype(jnp.bfloat16)
        got = lax.all_to_all(send_head, "sg", split_axis=0, concat_axis=0, tiled=True)
        taken_all = got[src_group[:, head]]
        part_count = 2 if head == head_count - 1 else 1
        step = slices // part_count
        att_parts = []
        qg_parts = []
        send_parts = []
        own_rows = []
        for part in range(part_count):
            lo = part * step
            hi = lo + step
            taken = taken_all[lo:hi]
            other = swap_pair(taken)
            sel_kv = jnp.stack([taken, other], axis=2)
            sel_kv = sel_kv.transpose(0, 3, 1, 2, 4, 5).reshape(step, 2, 2 * topk * half_len, HD)
            every_kv = jnp.concatenate([own_kv[lo:hi, :, head], sel_kv], axis=2)
            visible = jnp.concatenate(
                [
                    own_vis[lo:hi],
                    jnp.broadcast_to(
                        sel_vis[lo:hi, head, None, :], (step, half_len, sel_vis.shape[2])
                    ),
                ],
                axis=-1,
            )
            attended, query_gradient, terms = lax.map(
                attend,
                (
                    q_heads[head, lo:hi],
                    every_kv[:, 0],
                    every_kv[:, 1],
                    g_heads[head, lo:hi],
                    visible,
                ),
            )
            sel_terms = terms[:, :, block_len:].reshape(step, 2, topk, 2, half_len, HD)
            mine_terms = sel_terms[:, :, :, 0]
            other_terms = sel_terms[:, :, :, 1].astype(jnp.bfloat16)
            by_pair = terms[:, :, :half_len].reshape(step // 2, 2, 2, half_len, HD)
            trail = jnp.where(parity == 0, by_pair[:, 1], by_pair[:, 0]).astype(jnp.bfloat16)
            item_count = other_terms.size // (half_len * HD)
            both = jnp.concatenate(
                [other_terms.reshape(item_count, half_len, HD), trail.reshape(-1, half_len, HD)]
            )
            both = swap_pair(both)
            partner_terms = both[:item_count].reshape(other_terms.shape)
            mate_back = both[item_count:].reshape(trail.shape)
            summed = (mine_terms + partner_terms.astype(jnp.float32)).astype(jnp.bfloat16)
            route = (
                (src_group[None, lo:hi, head] == gid[:, None, None])
                & mine_usable[None, lo:hi, head]
            ).astype(jnp.bfloat16)
            send_parts.append(
                jnp.einsum("gfj,fcjld->gcld", route, summed, preferred_element_type=jnp.float32)
            )
            for local_id in range(step):
                first = terms[local_id, :, :half_len] + mate_back[local_id // 2].astype(
                    jnp.float32
                )
                second = terms[local_id, :, half_len:block_len]
                own_rows.append(jnp.where(held_half[lo + local_id] == 0, first, second))
            att_parts.append(attended)
            qg_parts.append(query_gradient)
        outgoing.append(sum(send_parts[1:], send_parts[0]).astype(jnp.bfloat16))
        owned.append(jnp.stack(own_rows, axis=1))
        attended_heads.append(jnp.concatenate(att_parts))
        query_heads.append(jnp.concatenate(qg_parts))

    back = lax.all_to_all(jnp.stack(outgoing, axis=2), "sg", split_axis=0, concat_axis=0, tiled=True)
    gathered = jnp.einsum("ghf,gchld->chfld", need, back, preferred_element_type=jnp.float32)
    grads = (jnp.stack(owned, axis=1) + gathered).astype(jnp.bfloat16)
    return (
        merge_heads(jnp.stack(attended_heads)),
        merge_heads(jnp.stack(query_heads)),
        merge_heads(grads[0]),
        merge_heads(grads[1]),
    )


def solution(mesh):
    seq_count = mesh.shape["seq"]
    head_count = mesh.shape["head"]
    pair_mesh = Mesh(
        mesh.devices.reshape(seq_count // 2, 2, head_count), ("sg", "sp", "head")
    )
    tokens = P(None, ("sg", "sp"), "head")
    in_specs = (
        tokens,
        tokens,
        tokens,
        P(None, ("sg", "sp", "head"), None),
        P(None, None, "head", None),
    )
    out_specs = (tokens, tokens, tokens, tokens)
    return jax.shard_map(
        layer, mesh=pair_mesh, in_specs=in_specs, out_specs=out_specs, check_vma=False
    )
```

```python
import math

import jax
import jax.numpy as jnp
from jax import lax
from jax.sharding import Mesh, PartitionSpec as P


HD = 128


def swap_pair(value):
    return lax.ppermute(value, "sp", [(0, 1), (1, 0)])


def per_head(stored, head_count):
    slices = stored.shape[0]
    rows = stored.shape[1]
    return stored.reshape(slices, rows, head_count, HD).transpose(2, 0, 1, 3)


def merge_heads(split):
    head_count = split.shape[0]
    slices = split.shape[1]
    rows = split.shape[2]
    return split.transpose(1, 2, 0, 3).reshape(slices, rows, head_count * HD)


def layer(queries, keys, values, out_grad, selected):
    groups = lax.axis_size("sg")
    seq_count = 2 * groups
    group_id = lax.axis_index("sg")
    parity = lax.axis_index("sp")
    slices = queries.shape[0]
    half_len = queries.shape[1]
    block_len = 2 * half_len
    head_count = queries.shape[2] // HD
    logit_scale_factor = 1.0 / math.sqrt(HD)
    q_heads = per_head(queries, head_count)
    k_heads = per_head(keys, head_count)
    v_heads = per_head(values, head_count)
    grad_rows = lax.all_to_all(out_grad, "head", split_axis=2, concat_axis=1, tiled=True)
    g_heads = per_head(grad_rows, head_count)
    kv = jnp.stack([k_heads, v_heads])

    sel_g = selected[:, 0::2]
    gid = jnp.arange(groups, dtype=jnp.int32)
    query_block = jnp.stack([gid, seq_count - 1 - gid, seq_count + gid, 2 * seq_count - 1 - gid])
    usable_g = sel_g < query_block[:, :, None, None]
    mine_block = jnp.stack(
        [group_id, seq_count - 1 - group_id, seq_count + group_id, 2 * seq_count - 1 - group_id]
    )
    hits = usable_g[..., None] & (sel_g[..., None] == mine_block)
    need = jnp.any(hits, axis=(0, 3)).astype(jnp.bfloat16)
    mine_sel = lax.dynamic_index_in_dim(sel_g, group_id, 1, keepdims=False)
    mine_usable = mine_sel < mine_block[:, None, None]
    fold = mine_sel % seq_count
    src_group = jnp.where(fold >= groups, seq_count - 1 - fold, fold)
    src_group = jnp.where(mine_usable, src_group, 0)

    send = jnp.einsum(
        "ghf,chfld->gchld", need, kv, preferred_element_type=jnp.float32
    ).astype(jnp.bfloat16)
    held_half = (jnp.arange(slices, dtype=jnp.int32) + parity) % 2
    pairs_kv = kv.reshape(2, head_count, slices // 2, 2, half_len, HD)
    lead = jnp.where(parity == 0, pairs_kv[:, :, :, 0], pairs_kv[:, :, :, 1])
    mate = swap_pair(lead)

    empty_span = jnp.zeros((2, head_count, half_len, HD), jnp.bfloat16)
    own_rows = []
    for slice_id in range(slices):
        second = jnp.concatenate([mate[:, :, slice_id // 2], kv[:, :, slice_id]], axis=2)
        first = jnp.concatenate([kv[:, :, slice_id], empty_span], axis=2)
        own_rows.append(jnp.where(held_half[slice_id] == 1, second, first))
    own_kv = jnp.stack(own_rows, axis=0)

    key_pos = jnp.arange(block_len, dtype=jnp.int32)
    query_pos = held_half[:, None] * half_len + jnp.arange(half_len, dtype=jnp.int32)[None, :]
    own_vis = key_pos[None, None, :] <= query_pos[:, :, None]
    sel_vis = jnp.repeat(mine_usable, block_len, axis=2)
    topk = sel_g.shape[3]

    def attend(operands):
        q_one, k_one, v_one, g_one, vis_one = operands
        attention_logits = (
            jnp.einsum("qd,kd->qk", q_one, k_one, preferred_element_type=jnp.float32)
            * logit_scale_factor
        )
        masked = jnp.where(vis_one, attention_logits, -jnp.inf)
        row_max = jnp.max(masked, axis=-1, keepdims=True)
        exp_vals = jnp.exp(masked - row_max)
        probs = exp_vals / jnp.sum(exp_vals, axis=-1, keepdims=True)
        probability_narrow = probs.astype(jnp.bfloat16)
        attended = jnp.einsum(
            "qk,kd->qd", probability_narrow, v_one, preferred_element_type=jnp.float32
        ).astype(jnp.bfloat16)
        probability_gradient = jnp.einsum(
            "qd,kd->qk", g_one, v_one, preferred_element_type=jnp.float32
        )
        row_delta = jnp.sum(probs * probability_gradient, axis=-1, keepdims=True)
        score_gradient = (probs * (probability_gradient - row_delta)).astype(jnp.bfloat16)
        query_gradient = (
            logit_scale_factor
            * jnp.einsum("qk,kd->qd", score_gradient, k_one, preferred_element_type=jnp.float32)
        ).astype(jnp.bfloat16)
        key_terms = logit_scale_factor * jnp.einsum(
            "qk,qd->kd", score_gradient, q_one, preferred_element_type=jnp.float32
        )
        value_terms = jnp.einsum(
            "qk,qd->kd", probability_narrow, g_one, preferred_element_type=jnp.float32
        )
        return (attended, query_gradient, jnp.stack([key_terms, value_terms]))

    attended_heads = []
    query_heads = []
    outgoing = []
    owned = []
    for head in range(head_count):
        got = lax.all_to_all(send[:, :, head], "sg", split_axis=0, concat_axis=0, tiled=True)
        taken_all = got[src_group[:, head]]
        part_count = 2 if head == head_count - 1 else 1
        step = slices // part_count
        att_parts = []
        qg_parts = []
        send_parts = []
        own_rows = []
        for part in range(part_count):
            lo = part * step
            hi = lo + step
            taken = taken_all[lo:hi]
            other = swap_pair(taken)
            sel_kv = jnp.stack([taken, other], axis=2)
            sel_kv = sel_kv.transpose(0, 3, 1, 2, 4, 5).reshape(step, 2, 2 * topk * half_len, HD)
            every_kv = jnp.concatenate([own_kv[lo:hi, :, head], sel_kv], axis=2)
            visible = jnp.concatenate(
                [
                    own_vis[lo:hi],
                    jnp.broadcast_to(
                        sel_vis[lo:hi, head, None, :], (step, half_len, sel_vis.shape[2])
                    ),
                ],
                axis=-1,
            )
            attended, query_gradient, terms = lax.map(
                attend,
                (
                    q_heads[head, lo:hi],
                    every_kv[:, 0],
                    every_kv[:, 1],
                    g_heads[head, lo:hi],
                    visible,
                ),
            )
            sel_terms = terms[:, :, block_len:].reshape(step, 2, topk, 2, half_len, HD)
            mine_terms = sel_terms[:, :, :, 0]
            other_terms = sel_terms[:, :, :, 1].astype(jnp.bfloat16)
            by_pair = terms[:, :, :half_len].reshape(step // 2, 2, 2, half_len, HD)
            trail = jnp.where(parity == 0, by_pair[:, 1], by_pair[:, 0]).astype(jnp.bfloat16)
            item_count = other_terms.size // (half_len * HD)
            both = jnp.concatenate(
                [other_terms.reshape(item_count, half_len, HD), trail.reshape(-1, half_len, HD)]
            )
            both = swap_pair(both)
            partner_terms = both[:item_count].reshape(other_terms.shape)
            mate_back = both[item_count:].reshape(trail.shape)
            summed = (mine_terms + partner_terms.astype(jnp.float32)).astype(jnp.bfloat16)
            route = (
                (src_group[None, lo:hi, head] == gid[:, None, None])
                & mine_usable[None, lo:hi, head]
            ).astype(jnp.bfloat16)
            send_parts.append(
                jnp.einsum("gfj,fcjld->gcld", route, summed, preferred_element_type=jnp.float32)
            )
            for local_id in range(step):
                first = terms[local_id, :, :half_len] + mate_back[local_id // 2].astype(
                    jnp.float32
                )
                second = terms[local_id, :, half_len:block_len]
                own_rows.append(jnp.where(held_half[lo + local_id] == 0, first, second))
            att_parts.append(attended)
            qg_parts.append(query_gradient)
        outgoing.append(sum(send_parts[1:], send_parts[0]).astype(jnp.bfloat16))
        owned.append(jnp.stack(own_rows, axis=1))
        attended_heads.append(jnp.concatenate(att_parts))
        query_heads.append(jnp.concatenate(qg_parts))

    back = lax.all_to_all(jnp.stack(outgoing, axis=1), "sg", split_axis=0, concat_axis=0, tiled=True)
    gathered = jnp.einsum("ghf,ghcld->chfld", need, back, preferred_element_type=jnp.float32)
    grads = (jnp.stack(owned, axis=1) + gathered).astype(jnp.bfloat16)
    return (
        merge_heads(jnp.stack(attended_heads)),
        merge_heads(jnp.stack(query_heads)),
        merge_heads(grads[0]),
        merge_heads(grads[1]),
    )


def solution(mesh):
    seq_count = mesh.shape["seq"]
    head_count = mesh.shape["head"]
    pair_mesh = Mesh(
        mesh.devices.reshape(seq_count // 2, 2, head_count), ("sg", "sp", "head")
    )
    tokens = P(None, ("sg", "sp"), "head")
    in_specs = (
        tokens,
        tokens,
        tokens,
        P(None, ("sg", "sp", "head"), None),
        P(None, None, "head", None),
    )
    out_specs = (tokens, tokens, tokens, tokens)
    return jax.shard_map(
        layer, mesh=pair_mesh, in_specs=in_specs, out_specs=out_specs, check_vma=False
    )
```
